768 devices in a mesh: row: 64 (over y, x, core), col: 12 (over z).
Axes of the slice: x: 4, y: 8, z: 12, core: 2. Of those that a mesh axis runs over, the one named last changes fastest.
Arguments:
- qkv: bfloat16 [12, 8192, 1920], P('col', 'row'), may hold values from -20 to 20
- cotangent: bfloat16 [12, 8192, 1280], P('col', 'row'), may hold values from -6 to 6
- out_weight: bfloat16 [640, 1280], replicated, may hold values from -0.25 to 0.25
- live_patches: int32 [12, 64], P('col', 'row'), may hold values from 1 to 128, as said below
Outputs:
- output: bfloat16 [12, 8192, 1280], P('col', 'row')
- d_qkv: bfloat16 [12, 8192, 1920], P('col', 'row')
- d_weight: float32 [640, 1280], P('row')
The draws below stay inside these ranges and needn't reach their ends.
Inputs may be any that keep to these rules, and one draw needn't show every extreme that they name: `live_patches`: patches beyond a rank's count are padding; some rank holds 128 live patches.
All inputs are finite; a program needn't handle non-finite values.
Results may differ from the reference program's by a relative error of at most 0.007.
Values may be sent and summed in bfloat16 or wider, within the bound.
No kernel may reach another device: no remote copies, remote signals or barrier semaphores. Data moves between devices by JAX's collectives and lax.ppermute only.
A program may use at most 64 MiB of HBM per device.

```python
import jax
import jax.numpy as jnp
from jax import lax

D = 1280
HD = 80
H = 8
WIN = 64
W_DEV = 2
RANKS = 64
REPLICAS = 12
TOKENS = 8192


def draw_live_patches(key, part):
    largest = W_DEV * WIN
    key_level, key_fraction, key_force = jax.random.split(key, 3)
    levels_drawn = jax.random.randint(key_level, (REPLICAS, RANKS), 0, 3)
    ceiling = jnp.right_shift(jnp.full((REPLICAS, RANKS), largest, jnp.int32), levels_drawn)
    fraction = jax.random.randint(key_fraction, (REPLICAS, RANKS), 0, 1 << 20)
    counts = 1 + jnp.right_shift(fraction * ceiling, 20)
    forced = jax.random.randint(key_force, (), 0, REPLICAS * RANKS)
    flattened = jnp.where(jnp.arange(REPLICAS * RANKS) == forced, largest, counts.reshape(-1))
    return flattened.reshape(REPLICAS, RANKS).astype(jnp.int32)


def draw_qkv(key, part):
    key_base = jax.random.fold_in(key, 0)
    shape = (REPLICAS, TOKENS // WIN, WIN, H, 3, HD)
    drawn = jnp.clip(jax.random.normal(key_base, shape, jnp.float32), -6.0, 6.0)
    return drawn.reshape(REPLICAS, TOKENS, H * 3 * HD).astype(jnp.bfloat16)


def shard_levels(own_key, extent, pieces, least, high):
    def one(dim, blocks):
        steps = jax.random.uniform(jax.random.fold_in(jax.random.fold_in(own_key, 6), dim), (blocks,), jnp.float32, least / len(pieces), high / len(pieces))
        return jnp.repeat(jnp.exp(steps), extent[dim] // blocks).reshape((-1,) + (1,) * (len(extent) - dim - 1))

    loudness = one(*pieces[0])
    for cut in pieces[1:]:
        loudness = loudness * one(*cut)
    return loudness


def gaussian(key, dims, spread, bound, shards=(), kind=jnp.bfloat16):
    values = jax.random.normal(key, dims, jnp.float32) * spread
    if len(shards) > 0:
        values = shard_levels(key, dims, shards, -0.22, 0.18) * values
    return jnp.clip(values, min=-bound, max=bound).astype(kind)


def setup_inputs(seed: int = 0) -> dict:
    key_of = jax.random.split(jax.random.key(seed), 5)
    qkv = draw_qkv(jax.random.fold_in(key_of[4], 71), 0)
    cotangent = gaussian(key_of[1], (REPLICAS, TOKENS, D), 1.0, 6.0, ((0, 12), (1, 64)))
    out_weight = gaussian(key_of[2], (H * HD, D), (H * HD) ** -0.5, 0.25)
    live_patches = draw_live_patches(jax.random.fold_in(key_of[4], 71), 0)
    return dict(qkv=qkv, cotangent=cotangent, out_weight=out_weight, live_patches=live_patches)


def unit_attention(unit_block, keys_live):
    head_channels = unit_block.shape[-1] // 3
    window_len = unit_block.shape[1]
    query_matrix = unit_block[..., :head_channels].astype(jnp.float32)
    key_matrix = unit_block[..., head_channels:2 * head_channels].astype(jnp.float32)
    value_matrix = unit_block[..., 2 * head_channels:].astype(jnp.float32)
    places = jnp.arange(window_len, dtype=jnp.int32)
    key_alive = places[None, :] < keys_live[:, None]
    attention_logits = jnp.einsum('ohc,opc->ohp', query_matrix, key_matrix, precision=lax.Precision.HIGHEST) * head_channels ** (-0.5)
    attention_logits = jnp.where(key_alive[:, None, :], attention_logits, -1e+30)
    row_peak = lax.optimization_barrier(jnp.max(attention_logits, axis=-1, keepdims=True))
    weights = jnp.exp(attention_logits - row_peak)
    row_total = lax.optimization_barrier(jnp.sum(weights, axis=-1, keepdims=True))
    attention_probabilities = (weights / row_total).astype(jnp.bfloat16)
    attended_values = jnp.einsum('gcn,gnu->gcu', attention_probabilities.astype(jnp.float32), value_matrix, precision=lax.Precision.HIGHEST)
    attended_values = jnp.where(key_alive[:, :, None], attended_values, 0.0)
    return attended_values.astype(jnp.bfloat16)

def tokens_to_units(token_rows, head_channels):
    window_count = token_rows.shape[0] // WIN
    shaped = token_rows.reshape(window_count, WIN, H, head_channels)
    return shaped.transpose(0, 2, 1, 3).reshape(window_count * H, WIN, head_channels)

def units_to_tokens(unit_rows, head_channels):
    window_count = unit_rows.shape[0] // H
    shaped = unit_rows.reshape(window_count, H, WIN, head_channels)
    return shaped.transpose(0, 2, 1, 3).reshape(window_count * WIN, H * head_channels)

def reference(qkv, cotangent, out_weight, live_patches):

    def one_replica(replica):
        token_rows = qkv[replica]
        grad_rows = cotangent[replica]
        counts = live_patches[replica]
        all_units = tokens_to_units(token_rows, 3 * HD)
        unit_ids = jnp.arange(all_units.shape[0], dtype=jnp.int32)
        window_ids = unit_ids // H
        rank_ids = window_ids // W_DEV
        inner_ids = window_ids % W_DEV
        unit_live = jnp.clip(counts[rank_ids] - inner_ids * WIN, 0, WIN).astype(jnp.int32)
        attended_units, pullback = jax.vjp(lambda block_units: unit_attention(block_units, unit_live), all_units)
        attended_values = units_to_tokens(attended_units, HD)
        output = jnp.dot(attended_values, out_weight, preferred_element_type=jnp.float32).astype(jnp.bfloat16)
        grad_attended = lax.dot_general(grad_rows, out_weight, (((1,), (1,)), ((), ())), preferred_element_type=jnp.float32).astype(jnp.bfloat16)
        unit_grads, = pullback(tokens_to_units(grad_attended, HD))
        d_qkv = units_to_tokens(unit_grads, 3 * HD)
        weight_term = lax.dot_general(attended_values, grad_rows, (((0,), (0,)), ((), ())), preferred_element_type=jnp.float32)
        return (output, d_qkv, weight_term)
    outputs, grads, terms = lax.map(one_replica, jnp.arange(REPLICAS, dtype=jnp.int32))
    d_weight = lax.optimization_barrier(jnp.sum(terms, axis=0)) * (REPLICAS * TOKENS) ** (-0.5)
    return (outputs, grads, d_weight)
```

```python
import jax
import jax.numpy as jnp
from jax import lax
from jax.sharding import PartitionSpec as P

HD = 80
H = 8
WIN = 64
HIGHEST = lax.Precision.HIGHEST


def attend(qkv_rows, live):
    token_count = qkv_rows.shape[0]
    window_count = token_count // WIN
    blocks = qkv_rows.reshape(window_count, WIN, H, 3, HD).astype(jnp.float32)
    query = blocks[:, :, :, 0, :]
    key = blocks[:, :, :, 1, :]
    value = blocks[:, :, :, 2, :]
    slots = jnp.arange(token_count, dtype=jnp.int32).reshape(window_count, WIN)
    alive = slots < live
    logits = jnp.einsum("wphc,wqhc->whpq", query, key, precision=HIGHEST) * HD ** (-0.5)
    logits = jnp.where(alive[:, None, None, :], logits, -1e30)
    peak = lax.optimization_barrier(jnp.max(logits, axis=-1, keepdims=True))
    weights = jnp.exp(logits - peak)
    total = lax.optimization_barrier(jnp.sum(weights, axis=-1, keepdims=True))
    probs = (weights / total).astype(jnp.bfloat16)
    attended = jnp.einsum(
        "whpq,wqhc->wphc", probs.astype(jnp.float32), value, precision=HIGHEST
    )
    attended = jnp.where(alive[:, :, None, None], attended, 0.0)
    return attended.astype(jnp.bfloat16).reshape(token_count, H * HD)


def body(qkv, cotangent, out_weight, live_patches):
    token_count = qkv.shape[1]
    live = live_patches[0, 0]
    grad_rows = cotangent[0]
    attended, pullback = jax.vjp(lambda rows: attend(rows, live), qkv[0])
    grad_attended = lax.dot_general(
        grad_rows, out_weight, (((1,), (1,)), ((), ())), preferred_element_type=jnp.float32
    ).astype(jnp.bfloat16)
    (d_qkv,) = pullback(grad_attended)
    output = jnp.dot(attended, out_weight, preferred_element_type=jnp.float32).astype(
        jnp.bfloat16
    )
    row_share = lax.psum_scatter(
        lax.dot_general(
            attended, grad_rows, (((0,), (0,)), ((), ())), preferred_element_type=jnp.float32
        ),
        "row",
        scatter_dimension=0,
        tiled=True,
    )
    scale = (lax.axis_size("col") * lax.axis_size("row") * token_count) ** (-0.5)
    d_weight = lax.psum(row_share, "col") * scale
    return (output[None], d_qkv[None], d_weight)


def solution(mesh):
    in_specs = (P("col", "row", None), P("col", "row", None), P(), P("col", "row"))
    out_specs = (P("col", "row", None), P("col", "row", None), P("row", None))
    return jax.shard_map(body, mesh=mesh, in_specs=in_specs, out_specs=out_specs, check_vma=False)
```

```python
import jax
import jax.numpy as jnp
from jax import lax
from jax.sharding import PartitionSpec as P

HD = 80
H = 8
WIN = 64
HIGHEST = lax.Precision.HIGHEST


def attend(qkv_rows, live):
    token_count = qkv_rows.shape[0]
    window_count = token_count // WIN
    blocks = qkv_rows.reshape(window_count, WIN, H, 3, HD).astype(jnp.float32)
    query = blocks[:, :, :, 0, :]
    key = blocks[:, :, :, 1, :]
    value = blocks[:, :, :, 2, :]
    slots = jnp.arange(token_count, dtype=jnp.int32).reshape(window_count, WIN)
    alive = slots < live
    logits = jnp.einsum("wphc,wqhc->whpq", query, key, precision=HIGHEST) * HD ** (-0.5)
    logits = jnp.where(alive[:, None, None, :], logits, -1e30)
    peak = lax.optimization_barrier(jnp.max(logits, axis=-1, keepdims=True))
    weights = jnp.exp(logits - peak)
    total = lax.optimization_barrier(jnp.sum(weights, axis=-1, keepdims=True))
    probs = (weights / total).astype(jnp.bfloat16)
    attended = jnp.einsum(
        "whpq,wqhc->wphc", probs.astype(jnp.float32), value, precision=HIGHEST
    )
    attended = jnp.where(alive[:, :, None, None], attended, 0.0)
    return attended.astype(jnp.bfloat16).reshape(token_count, H * HD)


def bit_orders(steps):
    low = list(range(1, steps))
    split = min(2, steps - 1)
    return [0] + low, [0] + low[split:] + low[:split]


def reduce_rows(columns, grad_rows):
    rank_total = lax.axis_size("row")
    steps = rank_total.bit_length() - 1
    rank = lax.axis_index("row")
    odd = (rank & 1) == 1
    orders = bit_orders(steps)
    token_count, width = columns.shape
    share = width // rank_total

    shaped = columns.reshape((token_count,) + (2,) * steps + (share,))
    halves = []
    for parity, order in enumerate(orders):
        half = lax.index_in_dim(shaped, parity, steps, keepdims=False)
        axes = [1 + (steps - 1 - bit) for bit in order[1:]]
        halves.append(half.transpose([0] + axes + [steps]))
    arranged = jnp.stack(halves, axis=1).reshape(token_count, width)
    current = lax.dot_general(
        arranged, grad_rows, (((0,), (0,)), ((), ())), preferred_element_type=jnp.float32
    )
    current = current.reshape((2,) * steps + (share * grad_rows.shape[1],))
    for step in range(steps):
        even_bit, odd_bit = orders[0][step], orders[1][step]
        bit = jnp.where(odd, odd_bit, even_bit)
        mine = (rank >> bit) & 1
        keep = lax.dynamic_index_in_dim(current, mine, 0, keepdims=False)
        send = lax.dynamic_index_in_dim(current, 1 - mine, 0, keepdims=False)
        pairs = [
            (i, i ^ (1 << (odd_bit if i & 1 else even_bit))) for i in range(rank_total)
        ]
        current = keep + lax.ppermute(send, "row", pairs)
    return current.reshape(share, grad_rows.shape[1])


def body(qkv, cotangent, out_weight, live_patches):
    token_count = qkv.shape[1]
    live = live_patches[0, 0]
    grad_rows = cotangent[0]
    attended, pullback = jax.vjp(lambda rows: attend(rows, live), qkv[0])
    row_share = reduce_rows(attended, grad_rows)
    grad_attended = lax.dot_general(
        grad_rows, out_weight, (((1,), (1,)), ((), ())), preferred_element_type=jnp.float32
    ).astype(jnp.bfloat16)
    (d_qkv,) = pullback(grad_attended)
    output = jnp.dot(attended, out_weight, preferred_element_type=jnp.float32).astype(
        jnp.bfloat16
    )
    scale = (lax.axis_size("col") * lax.axis_size("row") * token_count) ** (-0.5)
    d_weight = lax.all_gather(row_share, "col", axis=0, tiled=False).sum(0) * scale
    return (output[None], d_qkv[None], d_weight)


def solution(mesh):
    in_specs = (P("col", "row", None), P("col", "row", None), P(), P("col", "row"))
    out_specs = (P("col", "row", None), P("col", "row", None), P("row", None))
    return jax.shard_map(body, mesh=mesh, in_specs=in_specs, out_specs=out_specs, check_vma=False)
```

```python
import jax
import jax.numpy as jnp
from jax import lax
from jax.sharding import PartitionSpec as P

HD = 80
H = 8
WIN = 64
HIGHEST = lax.Precision.HIGHEST


def attend(qkv_rows, live):
    token_count = qkv_rows.shape[0]
    window_count = token_count // WIN
    blocks = qkv_rows.reshape(window_count, WIN, H, 3, HD).astype(jnp.float32)
    query = blocks[:, :, :, 0, :]
    key = blocks[:, :, :, 1, :]
    value = blocks[:, :, :, 2, :]
    slots = jnp.arange(token_count, dtype=jnp.int32).reshape(window_count, WIN)
    alive = slots < live
    logits = jnp.einsum("wphc,wqhc->whpq", query, key, precision=HIGHEST) * HD ** (-0.5)
    logits = jnp.where(alive[:, None, None, :], logits, -1e30)
    peak = lax.optimization_barrier(jnp.max(logits, axis=-1, keepdims=True))
    weights = jnp.exp(logits - peak)
    total = lax.optimization_barrier(jnp.sum(weights, axis=-1, keepdims=True))
    probs = (weights / total).astype(jnp.bfloat16)
    attended = jnp.einsum(
        "whpq,wqhc->wphc", probs.astype(jnp.float32), value, precision=HIGHEST
    )
    attended = jnp.where(alive[:, :, None, None], attended, 0.0)
    return attended.astype(jnp.bfloat16).reshape(token_count, H * HD)


def bit_orders(steps):
    low = list(range(1, steps))
    split = min(2, steps - 1)
    return [0] + low, [0] + low[split:] + low[:split]


def reduce_rows(columns, grad_rows):
    rank_total = lax.axis_size("row")
    steps = rank_total.bit_length() - 1
    rank = lax.axis_index("row")
    odd = (rank & 1) == 1
    orders = bit_orders(steps)
    token_count, width = columns.shape
    share = width // rank_total

    shaped = columns.reshape((token_count,) + (2,) * steps + (share,))
    halves = []
    for parity, order in enumerate(orders):
        half = lax.index_in_dim(shaped, parity, steps, keepdims=False)
        axes = [1 + (steps - 1 - bit) for bit in order[1:]]
        halves.append(half.transpose([0] + axes + [steps]))
    arranged = jnp.stack(halves, axis=1).reshape(token_count, width)
    current = lax.dot_general(
        arranged, grad_rows, (((0,), (0,)), ((), ())), preferred_element_type=jnp.float32
    )
    for step in range(steps):
        even_bit, odd_bit = orders[0][step], orders[1][step]
        bit = jnp.where(odd, odd_bit, even_bit)
        mine = (rank >> bit) & 1
        half = current.shape[0] // 2
        keep = lax.dynamic_slice_in_dim(current, mine * half, half, axis=0)
        send = lax.dynamic_slice_in_dim(current, (1 - mine) * half, half, axis=0)
        pairs = [
            (i, i ^ (1 << (odd_bit if i & 1 else even_bit))) for i in range(rank_total)
        ]
        current = keep + lax.ppermute(send, "row", pairs)
    return current


def sum_cols(share):
    col_total = lax.axis_size("col")
    col = lax.axis_index("col")
    group = 1
    while group * 2 <= col_total and col_total % (group * 2) == 0:
        pairs = [(i, i ^ group) for i in range(col_total)]
        share = share + lax.ppermute(share, "col", pairs)
        group *= 2
    groups = col_total // group
    if groups == 1:
        return share
    parts = [share]
    for shift in range(1, groups):
        pairs = [(i, (i + shift * group) % col_total) for i in range(col_total)]
        parts.append(lax.ppermute(share, "col", pairs))
    mine = col // group
    total = None
    for target in range(groups):
        value = parts[0]
        for k in range(1, groups):
            value = jnp.where((mine - k) % groups == target, parts[k], value)
        total = value if total is None else total + value
    return total


def body(qkv, cotangent, out_weight, live_patches):
    token_count = qkv.shape[1]
    live = live_patches[0, 0]
    grad_rows = cotangent[0]
    attended, pullback = jax.vjp(lambda rows: attend(rows, live), qkv[0])
    row_share = reduce_rows(attended, grad_rows)
    grad_attended = lax.dot_general(
        grad_rows, out_weight, (((1,), (1,)), ((), ())), preferred_element_type=jnp.float32
    ).astype(jnp.bfloat16)
    (d_qkv,) = pullback(grad_attended)
    output = jnp.dot(attended, out_weight, preferred_element_type=jnp.float32).astype(
        jnp.bfloat16
    )
    scale = (lax.axis_size("col") * lax.axis_size("row") * token_count) ** (-0.5)
    d_weight = sum_cols(row_share) * scale
    return (output[None], d_qkv[None], d_weight)


def solution(mesh):
    in_specs = (P("col", "row", None), P("col", "row", None), P(), P("col", "row"))
    out_specs = (P("col", "row", None), P("col", "row", None), P("row", None))
    return jax.shard_map(body, mesh=mesh, in_specs=in_specs, out_specs=out_specs, check_vma=False)
```

```python
import jax
import jax.numpy as jnp
from jax import lax
from jax.sharding import PartitionSpec as P

HD = 80
H = 8
WIN = 64
HIGHEST = lax.Precision.HIGHEST


def attend(qkv_rows, live):
    token_count = qkv_rows.shape[0]
    window_count = token_count // WIN
    blocks = qkv_rows.reshape(window_count, WIN, H, 3, HD).astype(jnp.float32)
    query = blocks[:, :, :, 0, :]
    key = blocks[:, :, :, 1, :]
    value = blocks[:, :, :, 2, :]
    slots = jnp.arange(token_count, dtype=jnp.int32).reshape(window_count, WIN)
    alive = slots < live
    logits = jnp.einsum("wphc,wqhc->whpq", query, key, precision=HIGHEST) * HD ** (-0.5)
    logits = jnp.where(alive[:, None, None, :], logits, -1e30)
    peak = lax.optimization_barrier(jnp.max(logits, axis=-1, keepdims=True))
    weights = jnp.exp(logits - peak)
    total = lax.optimization_barrier(jnp.sum(weights, axis=-1, keepdims=True))
    probs = (weights / total).astype(jnp.bfloat16)
    attended = jnp.einsum(
        "whpq,wqhc->wphc", probs.astype(jnp.float32), value, precision=HIGHEST
    )
    attended = jnp.where(alive[:, :, None, None], attended, 0.0)
    return attended.astype(jnp.bfloat16).reshape(token_count, H * HD)


def bit_steps(steps):
    low = [tuple(range(1, min(3, steps)))] if steps > 1 else []
    high = [tuple(range(3, min(5, steps)))] if steps > 3 else []
    rest = [(bit,) for bit in range(5, steps)]
    return [(0,)] + low + high + rest, [(0,)] + high + low + rest


def spread(bits, delta):
    out = 0
    for k, bit in enumerate(bits):
        if (delta >> (len(bits) - 1 - k)) & 1:
            out |= 1 << bit
    return out


def reduce_rows(columns, grad_rows):
    rank_total = lax.axis_size("row")
    steps = rank_total.bit_length() - 1
    rank = lax.axis_index("row")
    odd = (rank & 1) == 1
    even_steps, odd_steps = bit_steps(steps)
    orders = [[bit for part in plan for bit in part] for plan in (even_steps, odd_steps)]
    token_count, width = columns.shape
    share = width // rank_total

    shaped = columns.reshape((token_count,) + (2,) * steps + (share,))
    halves = []
    for parity, order in enumerate(orders):
        half = lax.index_in_dim(shaped, parity, steps, keepdims=False)
        axes = [1 + (steps - 1 - bit) for bit in order[1:]]
        halves.append(half.transpose([0] + axes + [steps]))
    arranged = jnp.stack(halves, axis=1).reshape(token_count, width)
    current = lax.dot_general(
        arranged, grad_rows, (((0,), (0,)), ((), ())), preferred_element_type=jnp.float32
    )
    for even_bits, odd_bits in zip(even_steps, odd_steps):
        count = 1 << len(even_bits)
        mine = jnp.zeros((), jnp.int32)
        for k in range(len(even_bits)):
            bit = jnp.where(odd, odd_bits[k], even_bits[k])
            mine = mine | (((rank >> bit) & 1) << (len(even_bits) - 1 - k))
        part = current.shape[0] // count
        total = lax.dynamic_slice_in_dim(current, mine * part, part, axis=0)
        for delta in range(1, count):
            send = lax.dynamic_slice_in_dim(current, (mine ^ delta) * part, part, axis=0)
            pairs = [
                (i, i ^ spread(odd_bits if i & 1 else even_bits, delta))
                for i in range(rank_total)
            ]
            total = total + lax.ppermute(send, "row", pairs)
        current = total
    return current


def sum_cols(share):
    col_total = lax.axis_size("col")
    col = lax.axis_index("col")
    group = 4
    while col_total % group:
        group //= 2
    got = {0: share}
    for delta in range(1, group):
        got[delta] = lax.ppermute(share, "col", [(i, i ^ delta) for i in range(col_total)])
    own = col % group
    total = None
    for member in range(group):
        value = got[0]
        for delta in range(1, group):
            value = jnp.where((own ^ delta) == member, got[delta], value)
        total = value if total is None else total + value
    share = total
    groups = col_total // group
    if groups == 1:
        return share
    parts = [share]
    for shift in range(1, groups):
        pairs = [(i, (i + shift * group) % col_total) for i in range(col_total)]
        parts.append(lax.ppermute(share, "col", pairs))
    mine = col // group
    total = None
    for target in range(groups):
        value = parts[0]
        for k in range(1, groups):
            value = jnp.where((mine - k) % groups == target, parts[k], value)
        total = value if total is None else total + value
    return total


def body(qkv, cotangent, out_weight, live_patches):
    token_count = qkv.shape[1]
    live = live_patches[0, 0]
    grad_rows = cotangent[0]
    attended, pullback = jax.vjp(lambda rows: attend(rows, live), qkv[0])
    row_share = reduce_rows(attended, grad_rows)
    grad_attended = lax.dot_general(
        grad_rows, out_weight, (((1,), (1,)), ((), ())), preferred_element_type=jnp.float32
    ).astype(jnp.bfloat16)
    (d_qkv,) = pullback(grad_attended)
    output = jnp.dot(attended, out_weight, preferred_element_type=jnp.float32).astype(
        jnp.bfloat16
    )
    scale = (lax.axis_size("col") * lax.axis_size("row") * token_count) ** (-0.5)
    d_weight = sum_cols(row_share) * scale
    return (output[None], d_qkv[None], d_weight)


def solution(mesh):
    in_specs = (P("col", "row", None), P("col", "row", None), P(), P("col", "row"))
    out_specs = (P("col", "row", None), P("col", "row", None), P("row", None))
    return jax.shard_map(body, mesh=mesh, in_specs=in_specs, out_specs=out_specs, check_vma=False)
```

```python
import jax
import jax.numpy as jnp
from jax import lax
from jax.sharding import PartitionSpec as P

HD = 80
H = 8
WIN = 64
HIGHEST = lax.Precision.HIGHEST


def attend(qkv_rows, live):
    token_count = qkv_rows.shape[0]
    window_count = token_count // WIN
    blocks = qkv_rows.reshape(window_count, WIN, H, 3, HD).astype(jnp.float32)
    query = blocks[:, :, :, 0, :]
    key = blocks[:, :, :, 1, :]
    value = blocks[:, :, :, 2, :]
    slots = jnp.arange(token_count, dtype=jnp.int32).reshape(window_count, WIN)
    alive = slots < live
    logits = jnp.einsum("wphc,wqhc->whpq", query, key, precision=HIGHEST) * HD ** (-0.5)
    logits = jnp.where(alive[:, None, None, :], logits, -1e30)
    peak = lax.optimization_barrier(jnp.max(logits, axis=-1, keepdims=True))
    weights = jnp.exp(logits - peak)
    total = lax.optimization_barrier(jnp.sum(weights, axis=-1, keepdims=True))
    probs = (weights / total).astype(jnp.bfloat16)
    attended = jnp.einsum(
        "whpq,wqhc->wphc", probs.astype(jnp.float32), value, precision=HIGHEST
    )
    attended = jnp.where(alive[:, :, None, None], attended, 0.0)
    return attended.astype(jnp.bfloat16).reshape(token_count, H * HD)


def bit_steps(steps):
    low = [tuple(range(1, min(3, steps)))] if steps > 1 else []
    high = [tuple(range(3, min(5, steps)))] if steps > 3 else []
    rest = [(bit,) for bit in range(5, steps)]
    return [(0,)] + low + high + rest, [(0,)] + high + low + rest


def spread(bits, delta):
    out = 0
    for k, bit in enumerate(bits):
        if (delta >> (len(bits) - 1 - k)) & 1:
            out |= 1 << bit
    return out


def reduce_rows(columns, grad_rows):
    rank_total = lax.axis_size("row")
    steps = rank_total.bit_length() - 1
    rank = lax.axis_index("row")
    odd = (rank & 1) == 1
    even_steps, odd_steps = bit_steps(steps)
    orders = [[bit for part in plan for bit in part] for plan in (even_steps, odd_steps)]
    token_count, width = columns.shape
    share = width // rank_total

    shaped = columns.reshape((token_count,) + (2,) * steps + (share,))
    halves = []
    for parity, order in enumerate(orders):
        half = lax.index_in_dim(shaped, parity, steps, keepdims=False)
        axes = [1 + (steps - 1 - bit) for bit in order[1:]]
        halves.append(half.transpose([0] + axes + [steps]))
    arranged = jnp.stack(halves, axis=1).reshape(token_count, width)

    def product(index, count):
        part = width // count
        picked = lax.dynamic_slice_in_dim(arranged, index * part, part, axis=1)
        return lax.dot_general(
            picked, grad_rows, (((0,), (0,)), ((), ())), preferred_element_type=jnp.float32
        )

    half = (rank & 1).astype(jnp.int32)
    pairs = [(i, i ^ 1) for i in range(rank_total)]
    current = product(half, 2) + lax.ppermute(product(1 - half, 2), "row", pairs)
    for even_bits, odd_bits in zip(even_steps[1:], odd_steps[1:]):
        count = 1 << len(even_bits)
        mine = jnp.zeros((), jnp.int32)
        for k in range(len(even_bits)):
            bit = jnp.where(odd, odd_bits[k], even_bits[k])
            mine = mine | (((rank >> bit) & 1) << (len(even_bits) - 1 - k))
        part = current.shape[0] // count
        total = lax.dynamic_slice_in_dim(current, mine * part, part, axis=0)
        for delta in range(1, count):
            send = lax.dynamic_slice_in_dim(current, (mine ^ delta) * part, part, axis=0)
            pairs = [
                (i, i ^ spread(odd_bits if i & 1 else even_bits, delta))
                for i in range(rank_total)
            ]
            total = total + lax.ppermute(send, "row", pairs)
        current = total
    return current


def sum_cols(share):
    col_total = lax.axis_size("col")
    col = lax.axis_index("col")
    group = 4
    while col_total % group:
        group //= 2
    got = {0: share}
    for delta in range(1, group):
        got[delta] = lax.ppermute(share, "col", [(i, i ^ delta) for i in range(col_total)])
    own = col % group
    total = None
    for member in range(group):
        value = got[0]
        for delta in range(1, group):
            value = jnp.where((own ^ delta) == member, got[delta], value)
        total = value if total is None else total + value
    share = total
    groups = col_total // group
    if groups == 1:
        return share
    parts = [share]
    for shift in range(1, groups):
        pairs = [(i, (i + shift * group) % col_total) for i in range(col_total)]
        parts.append(lax.ppermute(share, "col", pairs))
    mine = col // group
    total = None
    for target in range(groups):
        value = parts[0]
        for k in range(1, groups):
            value = jnp.where((mine - k) % groups == target, parts[k], value)
        total = value if total is None else total + value
    return total


def body(qkv, cotangent, out_weight, live_patches):
    token_count = qkv.shape[1]
    live = live_patches[0, 0]
    grad_rows = cotangent[0]
    attended, pullback = jax.vjp(lambda rows: attend(rows, live), qkv[0])
    row_share = reduce_rows(attended, grad_rows)
    grad_attended = lax.dot_general(
        grad_rows, out_weight, (((1,), (1,)), ((), ())), preferred_element_type=jnp.float32
    ).astype(jnp.bfloat16)
    (d_qkv,) = pullback(grad_attended)
    output = jnp.dot(attended, out_weight, preferred_element_type=jnp.float32).astype(
        jnp.bfloat16
    )
    scale = (lax.axis_size("col") * lax.axis_size("row") * token_count) ** (-0.5)
    d_weight = sum_cols(row_share) * scale
    return (output[None], d_qkv[None], d_weight)


def solution(mesh):
    in_specs = (P("col", "row", None), P("col", "row", None), P(), P("col", "row"))
    out_specs = (P("col", "row", None), P("col", "row", None), P("row", None))
    return jax.shard_map(body, mesh=mesh, in_specs=in_specs, out_specs=out_specs, check_vma=False)
```

```python
import jax
import jax.numpy as jnp
from jax import lax
from jax.sharding import PartitionSpec as P

HD = 80
H = 8
WIN = 64
HIGHEST = lax.Precision.HIGHEST


def attend(qkv_rows, live):
    token_count = qkv_rows.shape[0]
    window_count = token_count // WIN
    blocks = qkv_rows.reshape(window_count, WIN, H, 3, HD).astype(jnp.float32)
    query = blocks[:, :, :, 0, :]
    key = blocks[:, :, :, 1, :]
    value = blocks[:, :, :, 2, :]
    slots = jnp.arange(token_count, dtype=jnp.int32).reshape(window_count, WIN)
    alive = slots < live
    logits = jnp.einsum("wphc,wqhc->whpq", query, key, precision=HIGHEST) * HD ** (-0.5)
    logits = jnp.where(alive[:, None, None, :], logits, -1e30)
    peak = lax.optimization_barrier(jnp.max(logits, axis=-1, keepdims=True))
    weights = jnp.exp(logits - peak)
    total = lax.optimization_barrier(jnp.sum(weights, axis=-1, keepdims=True))
    probs = (weights / total).astype(jnp.bfloat16)
    attended = jnp.einsum(
        "whpq,wqhc->wphc", probs.astype(jnp.float32), value, precision=HIGHEST
    )
    attended = jnp.where(alive[:, :, None, None], attended, 0.0)
    return attended.astype(jnp.bfloat16).reshape(token_count, H * HD)


def bit_steps(steps):
    low = [tuple(range(1, min(3, steps)))] if steps > 1 else []
    high = [tuple(range(4, min(6, steps)))] if steps > 4 else []
    rest = [(bit,) for bit in range(3, steps) if bit not in sum(high, ())]
    return [(0,)] + low + high + rest, [(0,)] + high + low + rest


def spread(bits, delta):
    out = 0
    for k, bit in enumerate(bits):
        if (delta >> (len(bits) - 1 - k)) & 1:
            out |= 1 << bit
    return out


def reduce_rows(columns, grad_rows):
    rank_total = lax.axis_size("row")
    steps = rank_total.bit_length() - 1
    rank = lax.axis_index("row")
    odd = (rank & 1) == 1
    even_steps, odd_steps = bit_steps(steps)
    orders = [[bit for part in plan for bit in part] for plan in (even_steps, odd_steps)]
    token_count, width = columns.shape
    share = width // rank_total

    shaped = columns.reshape((token_count,) + (2,) * steps + (share,))
    halves = []
    for parity, order in enumerate(orders):
        half = lax.index_in_dim(shaped, parity, steps, keepdims=False)
        axes = [1 + (steps - 1 - bit) for bit in order[1:]]
        halves.append(half.transpose([0] + axes + [steps]))
    arranged = jnp.stack(halves, axis=1).reshape(token_count, width)

    def product(index, count):
        part = width // count
        picked = lax.dynamic_slice_in_dim(arranged, index * part, part, axis=1)
        return lax.dot_general(
            picked, grad_rows, (((0,), (0,)), ((), ())), preferred_element_type=jnp.float32
        )

    half = (rank & 1).astype(jnp.int32)
    pairs = [(i, i ^ 1) for i in range(rank_total)]
    current = product(half, 2) + lax.ppermute(product(1 - half, 2), "row", pairs)
    for even_bits, odd_bits in zip(even_steps[1:], odd_steps[1:]):
        count = 1 << len(even_bits)
        mine = jnp.zeros((), jnp.int32)
        for k in range(len(even_bits)):
            bit = jnp.where(odd, odd_bits[k], even_bits[k])
            mine = mine | (((rank >> bit) & 1) << (len(even_bits) - 1 - k))
        part = current.shape[0] // count
        total = lax.dynamic_slice_in_dim(current, mine * part, part, axis=0)
        for delta in range(1, count):
            send = lax.dynamic_slice_in_dim(current, (mine ^ delta) * part, part, axis=0)
            pairs = [
                (i, i ^ spread(odd_bits if i & 1 else even_bits, delta))
                for i in range(rank_total)
            ]
            total = total + lax.ppermute(send, "row", pairs)
        current = total
    return current


def sum_cols(share):
    col_total = lax.axis_size("col")
    col = lax.axis_index("col")
    group = 4
    while col_total % group:
        group //= 2
    got = {0: share}
    for delta in range(1, group):
        got[delta] = lax.ppermute(share, "col", [(i, i ^ delta) for i in range(col_total)])
    own = col % group
    total = None
    for member in range(group):
        value = got[0]
        for delta in range(1, group):
            value = jnp.where((own ^ delta) == member, got[delta], value)
        total = value if total is None else total + value
    share = total
    groups = col_total // group
    if groups == 1:
        return share
    parts = [share]
    for shift in range(1, groups):
        pairs = [(i, (i + shift * group) % col_total) for i in range(col_total)]
        parts.append(lax.ppermute(share, "col", pairs))
    mine = col // group
    total = None
    for target in range(groups):
        value = parts[0]
        for k in range(1, groups):
            value = jnp.where((mine - k) % groups == target, parts[k], value)
        total = value if total is None else total + value
    return total


def body(qkv, cotangent, out_weight, live_patches):
    token_count = qkv.shape[1]
    live = live_patches[0, 0]
    grad_rows = cotangent[0]
    attended, pullback = jax.vjp(lambda rows: attend(rows, live), qkv[0])
    row_share = reduce_rows(attended, grad_rows)
    grad_attended = lax.dot_general(
        grad_rows, out_weight, (((1,), (1,)), ((), ())), preferred_element_type=jnp.float32
    ).astype(jnp.bfloat16)
    (d_qkv,) = pullback(grad_attended)
    output = jnp.dot(attended, out_weight, preferred_element_type=jnp.float32).astype(
        jnp.bfloat16
    )
    scale = (lax.axis_size("col") * lax.axis_size("row") * token_count) ** (-0.5)
    d_weight = sum_cols(row_share) * scale
    return (output[None], d_qkv[None], d_weight)


def solution(mesh):
    in_specs = (P("col", "row", None), P("col", "row", None), P(), P("col", "row"))
    out_specs = (P("col", "row", None), P("col", "row", None), P("row", None))
    return jax.shard_map(body, mesh=mesh, in_specs=in_specs, out_specs=out_specs, check_vma=False)
```

```python
import jax
import jax.numpy as jnp
from jax import lax
from jax.sharding import PartitionSpec as P

HD = 80
H = 8
WIN = 64
HIGHEST = lax.Precision.HIGHEST


def attend(qkv_rows, live):
    token_count = qkv_rows.shape[0]
    window_count = token_count // WIN
    blocks = qkv_rows.reshape(window_count, WIN, H, 3, HD).astype(jnp.float32)
    query = blocks[:, :, :, 0, :]
    key = blocks[:, :, :, 1, :]
    value = blocks[:, :, :, 2, :]
    slots = jnp.arange(token_count, dtype=jnp.int32).reshape(window_count, WIN)
    alive = slots < live
    logits = jnp.einsum("wphc,wqhc->whpq", query, key, precision=HIGHEST) * HD ** (-0.5)
    logits = jnp.where(alive[:, None, None, :], logits, -1e30)
    peak = lax.optimization_barrier(jnp.max(logits, axis=-1, keepdims=True))
    weights = jnp.exp(logits - peak)
    total = lax.optimization_barrier(jnp.sum(weights, axis=-1, keepdims=True))
    probs = (weights / total).astype(jnp.bfloat16)
    attended = jnp.einsum(
        "whpq,wqhc->wphc", probs.astype(jnp.float32), value, precision=HIGHEST
    )
    attended = jnp.where(alive[:, :, None, None], attended, 0.0)
    return attended.astype(jnp.bfloat16).reshape(token_count, H * HD)


def bit_steps(steps):
    low = [tuple(range(1, min(3, steps)))] if steps > 1 else []
    high = [tuple(range(3, min(5, steps)))] if steps > 3 else []
    rest = [(bit,) for bit in range(5, steps)]
    return [(0,)] + low + high + rest, [(0,)] + high + low + rest


def spread(bits, delta):
    out = 0
    for k, bit in enumerate(bits):
        if (delta >> (len(bits) - 1 - k)) & 1:
            out |= 1 << bit
    return out


def reduce_rows(columns, grad_rows):
    rank_total = lax.axis_size("row")
    steps = rank_total.bit_length() - 1
    rank = lax.axis_index("row")
    odd = (rank & 1) == 1
    even_steps, odd_steps = bit_steps(steps)
    orders = [[bit for part in plan for bit in part] for plan in (even_steps, odd_steps)]
    token_count, width = columns.shape
    share = width // rank_total

    shaped = columns.reshape((token_count,) + (2,) * steps + (share,))
    halves = []
    for parity, order in enumerate(orders):
        half = lax.index_in_dim(shaped, parity, steps, keepdims=False)
        axes = [1 + (steps - 1 - bit) for bit in order[1:]]
        halves.append(half.transpose([0] + axes + [steps]))
    arranged = jnp.stack(halves, axis=1).reshape(token_count, width)

    def product(index, count):
        part = width // count
        picked = lax.dynamic_slice_in_dim(arranged, index * part, part, axis=1)
        return lax.dot_general(
            picked, grad_rows, (((0,), (0,)), ((), ())), preferred_element_type=jnp.float32
        )

    half = (rank & 1).astype(jnp.int32)
    pairs = [(i, i ^ 1) for i in range(rank_total)]
    current = product(half, 2) + lax.ppermute(product(1 - half, 2), "row", pairs)
    for even_bits, odd_bits in zip(even_steps[1:], odd_steps[1:]):
        count = 1 << len(even_bits)
        mine = jnp.zeros((), jnp.int32)
        for k in range(len(even_bits)):
            bit = jnp.where(odd, odd_bits[k], even_bits[k])
            mine = mine | (((rank >> bit) & 1) << (len(even_bits) - 1 - k))
        part = current.shape[0] // count
        total = lax.dynamic_slice_in_dim(current, mine * part, part, axis=0)
        for delta in range(count - 1, 0, -1):
            send = lax.dynamic_slice_in_dim(current, (mine ^ delta) * part, part, axis=0)
            pairs = [
                (i, i ^ spread(odd_bits if i & 1 else even_bits, delta))
                for i in range(rank_total)
            ]
            total = total + lax.ppermute(send, "row", pairs)
        current = total
    return current


def sum_cols(share):
    col_total = lax.axis_size("col")
    col = lax.axis_index("col")
    group = 4
    while col_total % group:
        group //= 2
    got = {0: share}
    for delta in range(1, group):
        got[delta] = lax.ppermute(share, "col", [(i, i ^ delta) for i in range(col_total)])
    own = col % group
    total = None
    for member in range(group):
        value = got[0]
        for delta in range(1, group):
            value = jnp.where((own ^ delta) == member, got[delta], value)
        total = value if total is None else total + value
    share = total
    groups = col_total // group
    if groups == 1:
        return share
    parts = [share]
    for shift in range(1, groups):
        pairs = [(i, (i + shift * group) % col_total) for i in range(col_total)]
        parts.append(lax.ppermute(share, "col", pairs))
    mine = col // group
    total = None
    for target in range(groups):
        value = parts[0]
        for k in range(1, groups):
            value = jnp.where((mine - k) % groups == target, parts[k], value)
        total = value if total is None else total + value
    return total


def body(qkv, cotangent, out_weight, live_patches):
    token_count = qkv.shape[1]
    live = live_patches[0, 0]
    grad_rows = cotangent[0]
    attended, pullback = jax.vjp(lambda rows: attend(rows, live), qkv[0])
    row_share = reduce_rows(attended, grad_rows)
    grad_attended = lax.dot_general(
        grad_rows, out_weight, (((1,), (1,)), ((), ())), preferred_element_type=jnp.float32
    ).astype(jnp.bfloat16)
    (d_qkv,) = pullback(grad_attended)
    output = jnp.dot(attended, out_weight, preferred_element_type=jnp.float32).astype(
        jnp.bfloat16
    )
    scale = (lax.axis_size("col") * lax.axis_size("row") * token_count) ** (-0.5)
    d_weight = sum_cols(row_share) * scale
    return (output[None], d_qkv[None], d_weight)


def solution(mesh):
    in_specs = (P("col", "row", None), P("col", "row", None), P(), P("col", "row"))
    out_specs = (P("col", "row", None), P("col", "row", None), P("row", None))
    return jax.shard_map(body, mesh=mesh, in_specs=in_specs, out_specs=out_specs, check_vma=False)
```
